128 devices in a mesh: row: 8 (over z, core), col: 16 (over x, y).
Axes of the slice: x: 4, y: 4, z: 4, core: 2. Of those that a mesh axis runs over, the one named last changes fastest.
Arguments:
- updates: float32 [16384, 8192], P('col', 'row'), may hold values from -6 to 6
- block_map: int32 [2, 64], replicated, may hold values from 0 to 79, as said below
- own_diag: float32 [10240], P('row'), may hold values from 2 to 6
- panel_inverse: float32 [512, 512], replicated, as said below
Outputs:
- factor_panel: float32 [10240, 512], P('row')
- trailing: float32 [10240, 10240], P('row', 'col')
The draws below stay inside these ranges and needn't reach their ends.
Inputs may be any that keep to these rules, and one draw needn't show every extreme that they name: `block_map`: within one child the 64 entries name distinct front blocks. Take the child blocks (a, b) held by one device in updates, and the front blocks held by one device in trailing: either exactly 1 of the former land in the latter, or none do. `panel_inverse`: lower triangular with a positive diagonal.
All inputs are finite; a program needn't handle non-finite values.
Results may differ from the reference program's by a relative error of at most 0.000075.
Values sent between devices are 32-bit elements; how exact they have to be, the bound alone decides.
No kernel may reach another device: no remote copies, remote signals or barrier semaphores. Data moves between devices by JAX's collectives and lax.ppermute only.
A program may use at most 128 MiB of HBM per device.

```python
import math
import jax
import jax.numpy as jnp
from jax import lax

F = 10240
M = 8192
BLK = 128
PANEL = 512
MB = 64
N_ROW = 8
N_COL = 16


def draw_block_map(key, part):
    front_blocks = F // BLK
    col_blocks = front_blocks // N_COL
    per_col = MB // N_COL
    ratio = N_COL // N_ROW

    def child_draw(child_key):
        row_key, sub_key, slot_base = jax.random.split(child_key, 3)
        row_order = jax.random.permutation(row_key, N_ROW)
        sub_order = jax.random.permutation(sub_key, ratio)
        residue = jnp.arange(N_COL, dtype=jnp.int32)
        col_owner_of = row_order[residue % N_ROW] * ratio + sub_order[residue // N_ROW]
        slot_keys = jax.random.split(slot_base, N_COL)
        offsets = jax.vmap(lambda slot_key: jax.random.permutation(slot_key, col_blocks)[:per_col])(slot_keys)
        child_block = jnp.arange(MB, dtype=jnp.int32)
        owner_col = col_owner_of[child_block % N_COL]
        within = offsets[owner_col, child_block // N_COL]
        return (owner_col * col_blocks + within).astype(jnp.int32)
    return jnp.stack([child_draw(jax.random.fold_in(key, 11)), child_draw(jax.random.fold_in(key, 23))])


def draw_panel_inverse(key, part):
    lower_key, diag_key = jax.random.split(key)
    lower_part = jax.random.normal(lower_key, (PANEL, PANEL), jnp.float32)
    diag_part = jax.random.uniform(diag_key, (PANEL,), jnp.float32, 0.1, 0.3)
    row_ids = jnp.arange(PANEL)[:, None]
    col_ids = jnp.arange(PANEL)[None, :]
    strict_part = jnp.where(row_ids > col_ids, lower_part * (0.15 / math.sqrt(PANEL)), 0.0)
    return (strict_part + jnp.where(row_ids == col_ids, diag_part[None, :], 0.0)).astype(jnp.float32)


def level_of(key, dims, cuts, low, top_value):
    def one(axis_at, blocks):
        draws = jax.random.uniform(jax.random.fold_in(jax.random.fold_in(key, 6), axis_at), (blocks,), jnp.float32, low / len(cuts), top_value / len(cuts))
        return jnp.repeat(jnp.exp(draws), dims[axis_at] // blocks).reshape((-1,) + (1,) * (len(dims) - axis_at - 1))

    loudness = one(*cuts[0])
    for cut in cuts[1:]:
        loudness = loudness * one(*cut)
    return loudness


def centred(key, shape, spread, reach, pieces=(), kind=jnp.bfloat16):
    array = spread * jax.random.normal(key, shape, jnp.float32)
    if pieces:
        array = array * level_of(key, shape, pieces, -0.22, 0.18)
    return jnp.clip(array, -reach, reach).astype(kind)


def setup_inputs(seed: int = 0) -> dict:
    keys = jax.random.split(jax.random.key(seed), 5)
    return {
        "updates": centred(keys[0], (2 * M, M), 1.0, 6.0, ((0, 16), (1, 8)), jnp.float32),
        "block_map": draw_block_map(jax.random.fold_in(keys[4], 71), 0),
        "own_diag": jnp.clip(2.0 + 4.0 * jax.random.uniform(keys[2], (F,), jnp.float32) ** level_of(keys[2], (F,), ((0, 8),), -0.2, 0.2), 2.0, 6.0),
        "panel_inverse": draw_panel_inverse(jax.random.fold_in(keys[4], 71), 0),
    }


def reference(updates, block_map, own_diag, panel_inverse):
    blocks = F // BLK
    front_full = jnp.zeros((blocks, blocks, BLK, BLK), jnp.float32)
    for child_id in range(2):
        child_tiles = updates[child_id * M:(child_id + 1) * M].reshape(MB, BLK, MB, BLK).transpose(0, 2, 1, 3)
        mapping = block_map[child_id].astype(jnp.int32)
        front_full = front_full.at[mapping[:, None], mapping[None, :]].add(child_tiles)
    front_full = front_full.transpose(0, 2, 1, 3).reshape(F, F) + jnp.diag(own_diag)
    factor_panel = jnp.dot(front_full[:, :PANEL], panel_inverse.T, precision=lax.Precision.HIGHEST, preferred_element_type=jnp.float32)
    trailing = front_full - jnp.dot(factor_panel, factor_panel.T, precision=lax.Precision.HIGHEST, preferred_element_type=jnp.float32)
    return factor_panel, trailing
```

```python
import jax
import jax.numpy as jnp
from jax import lax
from jax.sharding import PartitionSpec as P

F = 10240
M = 8192
BLK = 128
PANEL = 512


def broadcast(shard, axis, root):
    mine = lax.axis_index(axis) == root
    return lax.psum(jnp.where(mine, shard, jnp.zeros_like(shard)), axis)


def item_routes(source_row, source_col, block_map, row_count, col_count):
    half_cols = col_count // 2
    row_items = 2 * M // col_count // BLK
    col_items = M // row_count // BLK
    front_rows = F // BLK // row_count
    front_cols = F // BLK // col_count
    child_map = jnp.take(block_map, source_col // half_cols, axis=0)
    row_parent = jnp.take(
        child_map, source_col % half_cols * row_items + jnp.arange(row_items, dtype=jnp.int32)
    )
    col_parent = jnp.take(
        child_map, source_row * col_items + jnp.arange(col_items, dtype=jnp.int32)
    )
    target_dev = (
        (row_parent // front_rows)[:, None] * col_count + (col_parent // front_cols)[None, :]
    ).reshape(-1)
    target_blk = (
        (row_parent % front_rows)[:, None] * front_cols + (col_parent % front_cols)[None, :]
    ).reshape(-1)
    position = jnp.arange(target_dev.shape[0], dtype=jnp.int32)
    same_target = (target_dev[:, None] == target_dev[None, :]) & (
        position[:, None] > position[None, :]
    )
    ranking = jnp.sum(same_target.astype(jnp.int32), axis=1)
    return (target_dev, ranking, target_blk)


def on_device(updates, block_map, own_diag, panel_inverse):
    row_count = lax.axis_size("row")
    col_count = lax.axis_size("col")
    row_index = lax.axis_index("row")
    col_index = lax.axis_index("col")
    devices_all = row_count * col_count
    local_rows, local_cols = updates.shape
    row_items = local_rows // BLK
    col_items = local_cols // BLK
    capacity = max(1, row_items // row_count) * max(1, col_items // col_count)
    front_rows = F // BLK // row_count
    front_cols = F // BLK // col_count
    slot_total = devices_all * capacity
    target_dev, ranking, unused_blk = item_routes(
        row_index, col_index, block_map, row_count, col_count
    )
    child_tiles = (
        updates.reshape(row_items, BLK, col_items, BLK)
        .transpose(0, 2, 1, 3)
        .reshape(row_items * col_items, BLK, BLK)
    )
    outgoing = (
        jnp.zeros((slot_total, BLK, BLK), jnp.float32)
        .at[target_dev * capacity + ranking]
        .set(child_tiles)
    )
    incoming = lax.all_to_all(
        outgoing.reshape(devices_all, capacity, BLK, BLK),
        ("row", "col"),
        split_axis=0,
        concat_axis=0,
        tiled=True,
    )
    sources = jnp.arange(devices_all, dtype=jnp.int32)
    all_dev, all_rank, all_blk = jax.vmap(
        lambda source_row, source_col: item_routes(
            source_row, source_col, block_map, row_count, col_count
        )
    )(sources // col_count, sources % col_count)
    myself = row_index * col_count + col_index
    slot_of = jnp.where(all_dev == myself, sources[:, None] * capacity + all_rank, slot_total)
    dump_slot = front_rows * front_cols
    slot_target = (
        jnp.full((slot_total + 1,), dump_slot, jnp.int32)
        .at[slot_of.reshape(-1)]
        .set(all_blk.reshape(-1))
    )
    slot_target = slot_target[:slot_total]
    assembled = (
        jnp.zeros((dump_slot + 1, BLK, BLK), jnp.float32)
        .at[slot_target]
        .add(incoming.reshape(slot_total, BLK, BLK))
    )
    height = front_rows * BLK
    col_width = front_cols * BLK
    front_local = (
        assembled[:dump_slot]
        .reshape(front_rows, front_cols, BLK, BLK)
        .transpose(0, 2, 1, 3)
        .reshape(height, col_width)
    )
    row_global = row_index * height + jnp.arange(height, dtype=jnp.int32)
    col_global = col_index * col_width + jnp.arange(col_width, dtype=jnp.int32)
    front_local = front_local + jnp.where(
        row_global[:, None] == col_global[None, :], own_diag[:, None], 0.0
    )
    raw_panel = broadcast(front_local[:, :PANEL], "col", 0)
    factor_panel = jnp.dot(
        raw_panel,
        panel_inverse.T,
        precision=lax.Precision.HIGHEST,
        preferred_element_type=jnp.float32,
    )
    ratio = col_count // row_count
    pieces = height // col_width
    half = lax.dynamic_slice_in_dim(factor_panel, (col_index % pieces) * col_width, col_width, 0)
    pairs = [
        (r * col_count + t, (t // ratio) * col_count + r * ratio + t % ratio)
        for r in range(row_count)
        for t in range(col_count)
    ]
    across = lax.ppermute(half, ("row", "col"), pairs)
    update_term = lax.dot_general(
        factor_panel,
        across,
        (((1,), (1,)), ((), ())),
        precision=lax.Precision.HIGHEST,
        preferred_element_type=jnp.float32,
    )
    trailing = front_local - update_term
    return (factor_panel, trailing)


def solution(mesh):
    return jax.shard_map(
        on_device,
        mesh=mesh,
        in_specs=(P("col", "row"), P(), P("row"), P()),
        out_specs=(P("row", None), P("row", "col")),
        check_vma=False,
    )
```

```python
import jax
import jax.numpy as jnp
from jax import lax
from jax.sharding import PartitionSpec as P

F = 10240
M = 8192
BLK = 128
PANEL = 512


def broadcast(shard, axis, root):
    mine = lax.axis_index(axis) == root
    return lax.psum(jnp.where(mine, shard, jnp.zeros_like(shard)), axis)


def item_routes(source_row, source_col, block_map, row_count, col_count):
    half_cols = col_count // 2
    row_items = 2 * M // col_count // BLK
    col_items = M // row_count // BLK
    front_rows = F // BLK // row_count
    front_cols = F // BLK // col_count
    child_map = jnp.take(block_map, source_col // half_cols, axis=0)
    row_parent = jnp.take(
        child_map, source_col % half_cols * row_items + jnp.arange(row_items, dtype=jnp.int32)
    )
    col_parent = jnp.take(
        child_map, source_row * col_items + jnp.arange(col_items, dtype=jnp.int32)
    )
    target_dev = (
        (row_parent // front_rows)[:, None] * col_count + (col_parent // front_cols)[None, :]
    ).reshape(-1)
    target_blk = (
        (row_parent % front_rows)[:, None] * front_cols + (col_parent % front_cols)[None, :]
    ).reshape(-1)
    position = jnp.arange(target_dev.shape[0], dtype=jnp.int32)
    same_target = (target_dev[:, None] == target_dev[None, :]) & (
        position[:, None] > position[None, :]
    )
    ranking = jnp.sum(same_target.astype(jnp.int32), axis=1)
    return (target_dev, ranking, target_blk)


def on_device(updates, block_map, own_diag, panel_inverse):
    row_count = lax.axis_size("row")
    col_count = lax.axis_size("col")
    row_index = lax.axis_index("row")
    col_index = lax.axis_index("col")
    devices_all = row_count * col_count
    local_rows, local_cols = updates.shape
    row_items = local_rows // BLK
    col_items = local_cols // BLK
    capacity = max(1, row_items // row_count) * max(1, col_items // col_count)
    front_rows = F // BLK // row_count
    front_cols = F // BLK // col_count
    slot_total = devices_all * capacity
    target_dev, ranking, unused_blk = item_routes(
        row_index, col_index, block_map, row_count, col_count
    )
    child_tiles = (
        updates.reshape(row_items, BLK, col_items, BLK)
        .transpose(0, 2, 1, 3)
        .reshape(row_items * col_items, BLK, BLK)
    )
    outgoing = (
        jnp.zeros((slot_total, BLK, BLK), jnp.float32)
        .at[target_dev * capacity + ranking]
        .set(child_tiles)
    )
    incoming = lax.all_to_all(
        outgoing.reshape(devices_all, capacity, BLK, BLK),
        ("row", "col"),
        split_axis=0,
        concat_axis=0,
        tiled=True,
    )
    sources = jnp.arange(devices_all, dtype=jnp.int32)
    all_dev, all_rank, all_blk = jax.vmap(
        lambda source_row, source_col: item_routes(
            source_row, source_col, block_map, row_count, col_count
        )
    )(sources // col_count, sources % col_count)
    myself = row_index * col_count + col_index
    slot_of = jnp.where(all_dev == myself, sources[:, None] * capacity + all_rank, slot_total)
    dump_slot = front_rows * front_cols
    slot_target = (
        jnp.full((slot_total + 1,), dump_slot, jnp.int32)
        .at[slot_of.reshape(-1)]
        .set(all_blk.reshape(-1))
    )
    slot_target = slot_target[:slot_total]
    assembled = (
        jnp.zeros((dump_slot + 1, BLK, BLK), jnp.float32)
        .at[slot_target]
        .add(incoming.reshape(slot_total, BLK, BLK))
    )
    height = front_rows * BLK
    col_width = front_cols * BLK
    front_local = (
        assembled[:dump_slot]
        .reshape(front_rows, front_cols, BLK, BLK)
        .transpose(0, 2, 1, 3)
        .reshape(height, col_width)
    )
    row_global = row_index * height + jnp.arange(height, dtype=jnp.int32)
    col_global = col_index * col_width + jnp.arange(col_width, dtype=jnp.int32)
    front_local = front_local + jnp.where(
        row_global[:, None] == col_global[None, :], own_diag[:, None], 0.0
    )
    piece_rows = height // col_count
    raw_panel = front_local[:, :PANEL]
    piece = jnp.where(col_index == 0, raw_panel[:piece_rows], 0.0)
    for k in range(1, col_count):
        pairs = [(r * col_count, r * col_count + k) for r in range(row_count)]
        piece = piece + lax.ppermute(
            raw_panel[k * piece_rows:(k + 1) * piece_rows], ("row", "col"), pairs
        )
    factor_piece = jnp.dot(
        piece,
        panel_inverse.T,
        precision=lax.Precision.HIGHEST,
        preferred_element_type=jnp.float32,
    )
    factor_panel = lax.all_gather(factor_piece, "col", axis=0, tiled=True)
    ratio = col_count // row_count
    pairs = [
        (r * col_count + k, (k % row_count) * col_count + r * ratio + k // row_count)
        for r in range(row_count)
        for k in range(col_count)
    ]
    moved = lax.ppermute(factor_piece, ("row", "col"), pairs)
    across = lax.all_gather(moved, "row", axis=0, tiled=True)
    update_term = lax.dot_general(
        factor_panel,
        across,
        (((1,), (1,)), ((), ())),
        precision=lax.Precision.HIGHEST,
        preferred_element_type=jnp.float32,
    )
    trailing = front_local - update_term
    return (factor_panel, trailing)


def solution(mesh):
    return jax.shard_map(
        on_device,
        mesh=mesh,
        in_specs=(P("col", "row"), P(), P("row"), P()),
        out_specs=(P("row", None), P("row", "col")),
        check_vma=False,
    )
```

```python
import jax
import jax.numpy as jnp
from jax import lax
from jax.sharding import PartitionSpec as P

F = 10240
M = 8192
BLK = 128
PANEL = 512


def broadcast(shard, axis, root):
    mine = lax.axis_index(axis) == root
    return lax.psum(jnp.where(mine, shard, jnp.zeros_like(shard)), axis)


def on_device(updates, block_map, own_diag, panel_inverse):
    row_count = lax.axis_size("row")
    col_count = lax.axis_size("col")
    row_index = lax.axis_index("row")
    col_index = lax.axis_index("col")
    devices_all = row_count * col_count
    local_rows, local_cols = updates.shape
    row_items = local_rows // BLK
    col_items = local_cols // BLK
    half_cols = col_count // 2
    front_blocks = F // BLK
    front_rows = front_blocks // row_count
    front_cols = front_blocks // col_count
    height = front_rows * BLK
    col_width = front_cols * BLK
    block_map = block_map.astype(jnp.int32)
    child = col_index // half_cols
    child_map = jnp.take(block_map, child, axis=0)
    row_parent = lax.dynamic_slice_in_dim(child_map, col_index % half_cols * row_items, row_items)
    col_parent = lax.dynamic_slice_in_dim(child_map, row_index * col_items, col_items)
    inv_k = (
        jnp.zeros((row_count,), jnp.int32)
        .at[row_parent // front_rows]
        .set(jnp.arange(row_items, dtype=jnp.int32))
    )
    inv_l = (
        jnp.full((col_count,), -1, jnp.int32)
        .at[col_parent // front_cols]
        .set(jnp.arange(col_items, dtype=jnp.int32))
    )
    row_sorted = jnp.take(updates.reshape(row_items, BLK, local_cols), inv_k, axis=0)
    picked = jnp.take(
        row_sorted.reshape(row_count, BLK, col_items, BLK), jnp.maximum(inv_l, 0), axis=2
    )
    picked = jnp.where((inv_l >= 0)[None, None, :, None], picked, 0.0)
    outgoing = picked.transpose(0, 2, 1, 3).reshape(devices_all, 1, BLK, BLK)
    incoming = lax.all_to_all(
        outgoing, ("row", "col"), split_axis=0, concat_axis=0, tiled=True
    ).reshape(devices_all, BLK, BLK)
    slots = jnp.arange(front_blocks, dtype=jnp.int32)
    my_rows = row_index * front_rows + jnp.arange(front_rows, dtype=jnp.int32)
    my_cols = col_index * front_cols + jnp.arange(front_cols, dtype=jnp.int32)
    front_local = None
    for child_id in range(2):
        inverse = (
            jnp.full((front_blocks,), -1, jnp.int32)
            .at[block_map[child_id]]
            .set(jnp.arange(block_map.shape[1], dtype=jnp.int32))
        )
        a = jnp.take(inverse, my_rows)
        b = jnp.take(inverse, my_cols)
        source = (jnp.maximum(b, 0) // col_items)[None, :] * col_count + (
            child_id * half_cols + jnp.maximum(a, 0) // row_items
        )[:, None]
        valid = (a >= 0)[:, None] & (b >= 0)[None, :]
        part = jnp.take(incoming, source.reshape(-1), axis=0).reshape(
            front_rows, front_cols, BLK, BLK
        )
        part = jnp.where(valid[:, :, None, None], part, 0.0)
        front_local = part if front_local is None else front_local + part
    front_local = front_local.transpose(0, 2, 1, 3).reshape(height, col_width)
    row_global = row_index * height + jnp.arange(height, dtype=jnp.int32)
    col_global = col_index * col_width + jnp.arange(col_width, dtype=jnp.int32)
    front_local = front_local + jnp.where(
        row_global[:, None] == col_global[None, :], own_diag[:, None], 0.0
    )
    piece_rows = height // col_count
    raw_panel = front_local[:, :PANEL]
    piece = jnp.where(col_index == 0, raw_panel[:piece_rows], 0.0)
    for k in range(1, col_count):
        pairs = [(r * col_count, r * col_count + k) for r in range(row_count)]
        piece = piece + lax.ppermute(
            raw_panel[k * piece_rows:(k + 1) * piece_rows], ("row", "col"), pairs
        )
    factor_piece = jnp.dot(
        piece,
        panel_inverse.T,
        precision=lax.Precision.HIGHEST,
        preferred_element_type=jnp.float32,
    )
    factor_panel = lax.all_gather(factor_piece, "col", axis=0, tiled=True)
    ratio = col_count // row_count
    pairs = [
        (r * col_count + k, (k % row_count) * col_count + r * ratio + k // row_count)
        for r in range(row_count)
        for k in range(col_count)
    ]
    moved = lax.ppermute(factor_piece, ("row", "col"), pairs)
    across = lax.all_gather(moved, "row", axis=0, tiled=True)
    update_term = lax.dot_general(
        factor_panel,
        across,
        (((1,), (1,)), ((), ())),
        precision=lax.Precision.HIGHEST,
        preferred_element_type=jnp.float32,
    )
    trailing = front_local - update_term
    return (factor_panel, trailing)


def solution(mesh):
    return jax.shard_map(
        on_device,
        mesh=mesh,
        in_specs=(P("col", "row"), P(), P("row"), P()),
        out_specs=(P("row", None), P("row", "col")),
        check_vma=False,
    )
```

```python
import jax
import jax.numpy as jnp
from jax import lax
from jax.sharding import PartitionSpec as P

F = 10240
M = 8192
BLK = 128
PANEL = 512


def on_device(updates, block_map, own_diag, panel_inverse):
    row_count = lax.axis_size("row")
    col_count = lax.axis_size("col")
    row_index = lax.axis_index("row")
    col_index = lax.axis_index("col")
    local_rows, local_cols = updates.shape
    row_items = local_rows // BLK
    col_items = local_cols // BLK
    assert row_items == row_count
    half_cols = col_count // 2
    front_blocks = F // BLK
    front_rows = front_blocks // row_count
    front_cols = front_blocks // col_count
    height = front_rows * BLK
    col_width = front_cols * BLK
    panel_blocks = PANEL // BLK
    child_blocks = block_map.shape[1]
    block_map = block_map.astype(jnp.int32)
    child = col_index // half_cols
    child_map = jnp.take(block_map, child, axis=0)
    row_parent = lax.dynamic_slice_in_dim(child_map, col_index % half_cols * row_items, row_items)
    inv_k = (
        jnp.zeros((row_count,), jnp.int32)
        .at[row_parent // front_rows]
        .set(jnp.arange(row_items, dtype=jnp.int32))
    )
    sorted_rows = jnp.take(updates.reshape(row_items, BLK, local_cols), inv_k, axis=0)
    row_block = lax.all_to_all(sorted_rows, "row", split_axis=0, concat_axis=0, tiled=True)
    tiles = (
        row_block.reshape(row_count, BLK, col_items, BLK)
        .transpose(0, 2, 1, 3)
        .reshape(row_count * col_items, BLK, BLK)
    )
    inverses = [
        jnp.full((front_blocks,), child_blocks, jnp.int32)
        .at[block_map[c]]
        .set(jnp.arange(child_blocks, dtype=jnp.int32))
        for c in range(2)
    ]
    my_inverse = jnp.where(child == 0, inverses[0], inverses[1])
    by_front_col = jnp.take(tiles, my_inverse, axis=0, mode="fill", fill_value=0.0)
    panel_part = by_front_col[:panel_blocks].transpose(1, 0, 2).reshape(BLK, PANEL)
    panel_parts = lax.all_gather(panel_part, "col", axis=0, tiled=False)
    outgoing = by_front_col.reshape(col_count, front_cols, BLK, BLK)
    incoming = lax.all_to_all(outgoing, "col", split_axis=0, concat_axis=0, tiled=True)
    my_rows = row_index * front_rows + jnp.arange(front_rows, dtype=jnp.int32)
    sources = []
    for c in range(2):
        a = jnp.take(inverses[c], my_rows)
        sources.append(jnp.where(a < child_blocks, c * half_cols + a // row_items, col_count))
    row_global = row_index * height + jnp.arange(height, dtype=jnp.int32)
    panel_raw = None
    for src in sources:
        part = jnp.take(panel_parts, src, axis=0, mode="fill", fill_value=0.0)
        panel_raw = part if panel_raw is None else panel_raw + part
    panel_raw = panel_raw.reshape(height, PANEL)
    panel_raw = panel_raw + jnp.where(
        row_global[:, None] == jnp.arange(PANEL, dtype=jnp.int32)[None, :], own_diag[:, None], 0.0
    )
    factor_panel = jnp.dot(
        panel_raw,
        panel_inverse.T,
        precision=lax.Precision.HIGHEST,
        preferred_element_type=jnp.float32,
    )
    piece_rows = col_width // row_count
    ratio = col_count // row_count
    received = []
    for q in range(row_count):
        chunk = lax.dynamic_slice_in_dim(
            factor_panel, (col_index // row_count) * col_width + q * piece_rows, piece_rows, 0
        )
        pairs = [
            (
                r * col_count + t,
                ((t % row_count - q) % row_count) * col_count + r * ratio + t // row_count,
            )
            for r in range(row_count)
            for t in range(col_count)
        ]
        received.append(lax.ppermute(chunk, ("row", "col"), pairs))
    across = jnp.concatenate(received, axis=0)
    incoming = incoming.reshape(col_count, front_cols, BLK, BLK)
    front_tiles = None
    for src in sources:
        part = jnp.take(incoming, src, axis=0, mode="fill", fill_value=0.0)
        front_tiles = part if front_tiles is None else front_tiles + part
    front_local = front_tiles.transpose(0, 2, 1, 3).reshape(height, col_width)
    col_global = col_index * col_width + jnp.arange(col_width, dtype=jnp.int32)
    front_local = front_local + jnp.where(
        row_global[:, None] == col_global[None, :], own_diag[:, None], 0.0
    )
    update_term = lax.dot_general(
        factor_panel,
        across,
        (((1,), (1,)), ((), ())),
        precision=lax.Precision.HIGHEST,
        preferred_element_type=jnp.float32,
    )
    trailing = front_local - update_term
    return (factor_panel, trailing)


def solution(mesh):
    return jax.shard_map(
        on_device,
        mesh=mesh,
        in_specs=(P("col", "row"), P(), P("row"), P()),
        out_specs=(P("row", None), P("row", "col")),
        check_vma=False,
    )
```

```python
import jax
import jax.numpy as jnp
from jax import lax
from jax.sharding import PartitionSpec as P

F = 10240
M = 8192
BLK = 128
PANEL = 512


def on_device(updates, block_map, own_diag, panel_inverse):
    row_count = lax.axis_size("row")
    col_count = lax.axis_size("col")
    row_index = lax.axis_index("row")
    col_index = lax.axis_index("col")
    devices_all = row_count * col_count
    local_rows, local_cols = updates.shape
    row_items = local_rows // BLK
    col_items = local_cols // BLK
    half_cols = col_count // 2
    front_blocks = F // BLK
    front_rows = front_blocks // row_count
    front_cols = front_blocks // col_count
    height = front_rows * BLK
    col_width = front_cols * BLK
    block_map = block_map.astype(jnp.int32)
    child = col_index // half_cols
    child_map = jnp.take(block_map, child, axis=0)
    row_parent = lax.dynamic_slice_in_dim(child_map, col_index % half_cols * row_items, row_items)
    col_parent = lax.dynamic_slice_in_dim(child_map, row_index * col_items, col_items)
    inv_k = (
        jnp.zeros((row_count,), jnp.int32)
        .at[row_parent // front_rows]
        .set(jnp.arange(row_items, dtype=jnp.int32))
    )
    inv_l = (
        jnp.full((col_count,), -1, jnp.int32)
        .at[col_parent // front_cols]
        .set(jnp.arange(col_items, dtype=jnp.int32))
    )
    fill_l = jnp.where(inv_l >= 0, inv_l, col_items)
    outgoing = (
        updates.reshape(row_items, BLK, col_items, BLK)
        .at[inv_k[:, None], :, fill_l[None, :], :]
        .get(mode="fill", fill_value=0.0)
        .reshape(devices_all, 1, BLK, BLK)
    )
    incoming = lax.all_to_all(
        outgoing, ("row", "col"), split_axis=0, concat_axis=0, tiled=True
    ).reshape(devices_all, BLK, BLK)
    my_rows = row_index * front_rows + jnp.arange(front_rows, dtype=jnp.int32)
    my_cols = col_index * front_cols + jnp.arange(front_cols, dtype=jnp.int32)
    lanes = jnp.arange(BLK, dtype=jnp.int32)
    front_local = None
    for child_id in range(2):
        inverse = (
            jnp.full((front_blocks,), -1, jnp.int32)
            .at[block_map[child_id]]
            .set(jnp.arange(block_map.shape[1], dtype=jnp.int32))
        )
        a = jnp.take(inverse, my_rows)
        b = jnp.take(inverse, my_cols)
        source = (jnp.maximum(b, 0) // col_items)[None, :] * col_count + (
            child_id * half_cols + jnp.maximum(a, 0) // row_items
        )[:, None]
        valid = (a >= 0)[:, None] & (b >= 0)[None, :]
        source = jnp.where(valid, source, devices_all)
        part = incoming.at[source[:, None, :], lanes[None, :, None], :].get(
            mode="fill", fill_value=0.0
        )
        front_local = part if front_local is None else front_local + part
    front_local = front_local.reshape(height, col_width)
    row_global = row_index * height + jnp.arange(height, dtype=jnp.int32)
    col_global = col_index * col_width + jnp.arange(col_width, dtype=jnp.int32)
    front_local = front_local + jnp.where(
        row_global[:, None] == col_global[None, :], own_diag[:, None], 0.0
    )
    piece_rows = height // col_count
    raw_panel = front_local[:, :PANEL]
    piece = jnp.where(col_index == 0, raw_panel[:piece_rows], 0.0)
    for k in range(1, col_count):
        pairs = [(r * col_count, r * col_count + k) for r in range(row_count)]
        piece = piece + lax.ppermute(
            raw_panel[k * piece_rows:(k + 1) * piece_rows], ("row", "col"), pairs
        )
    factor_piece = jnp.dot(
        piece,
        panel_inverse.T,
        precision=lax.Precision.HIGHEST,
        preferred_element_type=jnp.float32,
    )
    factor_panel = lax.all_gather(factor_piece, "col", axis=0, tiled=True)
    ratio = col_count // row_count
    pairs = [
        (r * col_count + k, (k % row_count) * col_count + r * ratio + k // row_count)
        for r in range(row_count)
        for k in range(col_count)
    ]
    moved = lax.ppermute(factor_piece, ("row", "col"), pairs)
    stack = [moved]
    for q in range(1, row_count):
        shift = [(r, (r + q) % row_count) for r in range(row_count)]
        stack.append(lax.ppermute(moved, "row", shift))
    order = (row_index - jnp.arange(row_count, dtype=jnp.int32)) % row_count
    across = jnp.take(jnp.stack(stack), order, axis=0).reshape(col_width, PANEL)
    update_term = lax.dot_general(
        factor_panel,
        across,
        (((1,), (1,)), ((), ())),
        precision=lax.Precision.HIGHEST,
        preferred_element_type=jnp.float32,
    )
    trailing = front_local - update_term
    return (factor_panel, trailing)


def solution(mesh):
    return jax.shard_map(
        on_device,
        mesh=mesh,
        in_specs=(P("col", "row"), P(), P("row"), P()),
        out_specs=(P("row", None), P("row", "col")),
        check_vma=False,
    )
```

```python
import jax
import jax.numpy as jnp
from jax import lax
from jax.sharding import PartitionSpec as P

F = 10240
M = 8192
BLK = 128
PANEL = 512


def on_device(updates, block_map, own_diag, panel_inverse):
    row_count = lax.axis_size("row")
    col_count = lax.axis_size("col")
    row_index = lax.axis_index("row")
    col_index = lax.axis_index("col")
    devices_all = row_count * col_count
    local_rows, local_cols = updates.shape
    row_items = local_rows // BLK
    col_items = local_cols // BLK
    half_cols = col_count // 2
    front_blocks = F // BLK
    front_rows = front_blocks // row_count
    front_cols = front_blocks // col_count
    height = front_rows * BLK
    col_width = front_cols * BLK
    block_map = block_map.astype(jnp.int32)
    child = col_index // half_cols
    child_map = jnp.take(block_map, child, axis=0)
    row_parent = lax.dynamic_slice_in_dim(child_map, col_index % half_cols * row_items, row_items)
    col_parent = lax.dynamic_slice_in_dim(child_map, row_index * col_items, col_items)
    inv_k = (
        jnp.zeros((row_count,), jnp.int32)
        .at[row_parent // front_rows]
        .set(jnp.arange(row_items, dtype=jnp.int32))
    )
    inv_l = (
        jnp.full((col_count,), -1, jnp.int32)
        .at[col_parent // front_cols]
        .set(jnp.arange(col_items, dtype=jnp.int32))
    )
    local_tiles = (
        updates.reshape(row_items, BLK, col_items, BLK)
        .transpose(0, 2, 1, 3)
        .reshape(row_items * col_items, BLK, BLK)
    )
    slot_tile = jnp.where(
        (inv_l >= 0)[None, :], inv_k[:, None] * col_items + inv_l[None, :], row_items * col_items
    )
    outgoing = jnp.take(
        local_tiles, slot_tile.reshape(-1), axis=0, mode="fill", fill_value=0.0
    ).reshape(devices_all, 1, BLK, BLK)
    incoming = lax.all_to_all(
        outgoing, ("row", "col"), split_axis=0, concat_axis=0, tiled=True
    ).reshape(devices_all, BLK, BLK)
    my_rows = row_index * front_rows + jnp.arange(front_rows, dtype=jnp.int32)
    my_cols = col_index * front_cols + jnp.arange(front_cols, dtype=jnp.int32)
    front_local = None
    for child_id in range(2):
        inverse = (
            jnp.full((front_blocks,), -1, jnp.int32)
            .at[block_map[child_id]]
            .set(jnp.arange(block_map.shape[1], dtype=jnp.int32))
        )
        a = jnp.take(inverse, my_rows)
        b = jnp.take(inverse, my_cols)
        source = (jnp.maximum(b, 0) // col_items)[None, :] * col_count + (
            child_id * half_cols + jnp.maximum(a, 0) // row_items
        )[:, None]
        valid = (a >= 0)[:, None] & (b >= 0)[None, :]
        source = jnp.where(valid, source, devices_all)
        part = jnp.take(incoming, source.reshape(-1), axis=0, mode="fill", fill_value=0.0)
        front_local = part if front_local is None else front_local + part
    front_local = (
        front_local.reshape(front_rows, front_cols, BLK, BLK)
        .transpose(0, 2, 1, 3)
        .reshape(height, col_width)
    )
    row_global = row_index * height + jnp.arange(height, dtype=jnp.int32)
    col_global = col_index * col_width + jnp.arange(col_width, dtype=jnp.int32)
    front_local = front_local + jnp.where(
        row_global[:, None] == col_global[None, :], own_diag[:, None], 0.0
    )
    piece_rows = height // col_count
    raw_panel = front_local[:, :PANEL]
    piece = jnp.where(col_index == 0, raw_panel[:piece_rows], 0.0)
    for k in range(1, col_count):
        pairs = [(r * col_count, r * col_count + k) for r in range(row_count)]
        piece = piece + lax.ppermute(
            raw_panel[k * piece_rows:(k + 1) * piece_rows], ("row", "col"), pairs
        )
    factor_piece = jnp.dot(
        piece,
        panel_inverse.T,
        precision=lax.Precision.HIGHEST,
        preferred_element_type=jnp.float32,
    )
    factor_panel = lax.all_gather(factor_piece, "col", axis=0, tiled=True)
    ratio = col_count // row_count
    pairs = [
        (r * col_count + k, (k % row_count) * col_count + r * ratio + k // row_count)
        for r in range(row_count)
        for k in range(col_count)
    ]
    moved = lax.ppermute(factor_piece, ("row", "col"), pairs)
    stack = [moved]
    for q in range(1, row_count):
        shift = [(r, (r + q) % row_count) for r in range(row_count)]
        stack.append(lax.ppermute(moved, "row", shift))
    order = (row_index - jnp.arange(row_count, dtype=jnp.int32)) % row_count
    across = jnp.take(jnp.stack(stack), order, axis=0).reshape(col_width, PANEL)
    update_term = lax.dot_general(
        factor_panel,
        across,
        (((1,), (1,)), ((), ())),
        precision=lax.Precision.HIGHEST,
        preferred_element_type=jnp.float32,
    )
    trailing = front_local - update_term
    return (factor_panel, trailing)


def solution(mesh):
    return jax.shard_map(
        on_device,
        mesh=mesh,
        in_specs=(P("col", "row"), P(), P("row"), P()),
        out_specs=(P("row", None), P("row", "col")),
        check_vma=False,
    )
```

```python
import jax
import jax.numpy as jnp
from jax import lax
from jax.sharding import PartitionSpec as P

F = 10240
M = 8192
BLK = 128
PANEL = 512


def on_device(updates, block_map, own_diag, panel_inverse):
    row_count = lax.axis_size("row")
    col_count = lax.axis_size("col")
    row_index = lax.axis_index("row")
    col_index = lax.axis_index("col")
    devices_all = row_count * col_count
    local_rows, local_cols = updates.shape
    row_items = local_rows // BLK
    col_items = local_cols // BLK
    half_cols = col_count // 2
    front_blocks = F // BLK
    front_rows = front_blocks // row_count
    front_cols = front_blocks // col_count
    height = front_rows * BLK
    col_width = front_cols * BLK
    block_map = block_map.astype(jnp.int32)
    child = col_index // half_cols
    child_map = jnp.take(block_map, child, axis=0)
    row_parent = lax.dynamic_slice_in_dim(child_map, col_index % half_cols * row_items, row_items)
    col_parent = lax.dynamic_slice_in_dim(child_map, row_index * col_items, col_items)
    inv_k = (
        jnp.zeros((row_count,), jnp.int32)
        .at[row_parent // front_rows]
        .set(jnp.arange(row_items, dtype=jnp.int32))
    )
    inv_l = (
        jnp.full((col_count,), -1, jnp.int32)
        .at[col_parent // front_cols]
        .set(jnp.arange(col_items, dtype=jnp.int32))
    )
    local_tiles = (
        updates.reshape(row_items, BLK, col_items, BLK)
        .transpose(0, 2, 1, 3)
        .reshape(row_items * col_items, BLK, BLK)
    )
    slot_tile = jnp.where(
        (inv_l >= 0)[None, :], inv_k[:, None] * col_items + inv_l[None, :], row_items * col_items
    )
    local_tiles = jnp.concatenate([local_tiles, jnp.zeros((1, BLK, BLK), jnp.float32)], axis=0)
    outgoing = jnp.take(local_tiles, slot_tile.reshape(-1), axis=0, mode="clip").reshape(
        devices_all, 1, BLK, BLK
    )
    incoming = lax.all_to_all(
        outgoing, ("row", "col"), split_axis=0, concat_axis=0, tiled=True
    ).reshape(devices_all, BLK, BLK)
    my_rows = row_index * front_rows + jnp.arange(front_rows, dtype=jnp.int32)
    my_cols = col_index * front_cols + jnp.arange(front_cols, dtype=jnp.int32)
    sources = []
    for child_id in range(2):
        inverse = (
            jnp.full((front_blocks,), -1, jnp.int32)
            .at[block_map[child_id]]
            .set(jnp.arange(block_map.shape[1], dtype=jnp.int32))
        )
        a = jnp.take(inverse, my_rows)
        b = jnp.take(inverse, my_cols)
        source = (jnp.maximum(b, 0) // col_items)[None, :] * col_count + (
            child_id * half_cols + jnp.maximum(a, 0) // row_items
        )[:, None]
        valid = (a >= 0)[:, None] & (b >= 0)[None, :]
        sources.append(jnp.where(valid, source, devices_all))

    def assemble(width):
        total = None
        for source in sources:
            part = jnp.take(
                incoming, source[:, :width].reshape(-1), axis=0, mode="fill", fill_value=0.0
            )
            total = part if total is None else total + part
        return (
            total.reshape(front_rows, width, BLK, BLK)
            .transpose(0, 2, 1, 3)
            .reshape(height, width * BLK)
        )

    row_global = row_index * height + jnp.arange(height, dtype=jnp.int32)
    col_global = col_index * col_width + jnp.arange(col_width, dtype=jnp.int32)
    diag = jnp.where(row_global[:, None] == col_global[None, :], own_diag[:, None], 0.0)
    raw_panel = assemble(PANEL // BLK) + diag[:, :PANEL]
    front_local = assemble(front_cols) + diag
    piece_rows = height // col_count
    piece_rows = height // col_count
    piece = jnp.where(col_index == 0, raw_panel[:piece_rows], 0.0)
    for k in range(1, col_count):
        pairs = [(r * col_count, r * col_count + k) for r in range(row_count)]
        piece = piece + lax.ppermute(
            raw_panel[k * piece_rows:(k + 1) * piece_rows], ("row", "col"), pairs
        )
    factor_piece = jnp.dot(
        piece,
        panel_inverse.T,
        precision=lax.Precision.HIGHEST,
        preferred_element_type=jnp.float32,
    )
    factor_panel = lax.all_gather(factor_piece, "col", axis=0, tiled=True)
    ratio = col_count // row_count
    pairs = [
        (r * col_count + k, (k % row_count) * col_count + r * ratio + k // row_count)
        for r in range(row_count)
        for k in range(col_count)
    ]
    moved = lax.ppermute(factor_piece, ("row", "col"), pairs)
    stack = [moved]
    for q in range(1, row_count):
        shift = [(r, (r + q) % row_count) for r in range(row_count)]
        stack.append(lax.ppermute(moved, "row", shift))
    order = (row_index - jnp.arange(row_count, dtype=jnp.int32)) % row_count
    across = jnp.take(jnp.stack(stack), order, axis=0).reshape(col_width, PANEL)
    update_term = lax.dot_general(
        factor_panel,
        across,
        (((1,), (1,)), ((), ())),
        precision=lax.Precision.HIGHEST,
        preferred_element_type=jnp.float32,
    )
    trailing = front_local - update_term
    return (factor_panel, trailing)


def solution(mesh):
    return jax.shard_map(
        on_device,
        mesh=mesh,
        in_specs=(P("col", "row"), P(), P("row"), P()),
        out_specs=(P("row", None), P("row", "col")),
        check_vma=False,
    )
```

```python
import jax
import jax.numpy as jnp
from jax import lax
from jax.sharding import PartitionSpec as P

F = 10240
M = 8192
BLK = 128
PANEL = 512


def on_device(updates, block_map, own_diag, panel_inverse):
    row_count = lax.axis_size("row")
    col_count = lax.axis_size("col")
    row_index = lax.axis_index("row")
    col_index = lax.axis_index("col")
    devices_all = row_count * col_count
    local_rows, local_cols = updates.shape
    row_items = local_rows // BLK
    col_items = local_cols // BLK
    half_cols = col_count // 2
    front_blocks = F // BLK
    front_rows = front_blocks // row_count
    front_cols = front_blocks // col_count
    height = front_rows * BLK
    col_width = front_cols * BLK
    block_map = block_map.astype(jnp.int32)
    child = col_index // half_cols
    child_map = jnp.take(block_map, child, axis=0)
    row_parent = lax.dynamic_slice_in_dim(child_map, col_index % half_cols * row_items, row_items)
    col_parent = lax.dynamic_slice_in_dim(child_map, row_index * col_items, col_items)
    inv_k = (
        jnp.zeros((row_count,), jnp.int32)
        .at[row_parent // front_rows]
        .set(jnp.arange(row_items, dtype=jnp.int32))
    )
    inv_l = (
        jnp.full((col_count,), -1, jnp.int32)
        .at[col_parent // front_cols]
        .set(jnp.arange(col_items, dtype=jnp.int32))
    )
    local_tiles = (
        updates.reshape(row_items, BLK, col_items, BLK)
        .transpose(0, 2, 1, 3)
        .reshape(row_items * col_items, BLK, BLK)
    )
    slot_tile = jnp.where(
        (inv_l >= 0)[None, :], inv_k[:, None] * col_items + inv_l[None, :], row_items * col_items
    )
    local_tiles = jnp.concatenate([local_tiles, jnp.zeros((1, BLK, BLK), jnp.float32)], axis=0)
    outgoing = jnp.take(local_tiles, slot_tile.reshape(-1), axis=0, mode="clip").reshape(
        devices_all, 1, BLK, BLK
    )
    incoming = lax.all_to_all(
        outgoing, ("row", "col"), split_axis=0, concat_axis=0, tiled=True
    ).reshape(devices_all, BLK, BLK)
    my_rows = row_index * front_rows + jnp.arange(front_rows, dtype=jnp.int32)
    my_cols = col_index * front_cols + jnp.arange(front_cols, dtype=jnp.int32)
    sources = []
    for child_id in range(2):
        inverse = (
            jnp.full((front_blocks,), -1, jnp.int32)
            .at[block_map[child_id]]
            .set(jnp.arange(block_map.shape[1], dtype=jnp.int32))
        )
        a = jnp.take(inverse, my_rows)
        b = jnp.take(inverse, my_cols)
        source = (jnp.maximum(b, 0) // col_items)[None, :] * col_count + (
            child_id * half_cols + jnp.maximum(a, 0) // row_items
        )[:, None]
        valid = (a >= 0)[:, None] & (b >= 0)[None, :]
        sources.append(jnp.where(valid, source, devices_all))

    def assemble(width):
        total = None
        for source in sources:
            part = jnp.take(
                incoming, source[:, :width].reshape(-1), axis=0, mode="fill", fill_value=0.0
            )
            total = part if total is None else total + part
        return (
            total.reshape(front_rows, width, BLK, BLK)
            .transpose(0, 2, 1, 3)
            .reshape(height, width * BLK)
        )

    row_global = row_index * height + jnp.arange(height, dtype=jnp.int32)
    col_global = col_index * col_width + jnp.arange(col_width, dtype=jnp.int32)
    diag = jnp.where(row_global[:, None] == col_global[None, :], own_diag[:, None], 0.0)
    raw_panel = assemble(PANEL // BLK) + diag[:, :PANEL]
    front_local = assemble(front_cols) + diag
    piece_rows = height // col_count
    half_rows = piece_rows // 2
    factor_halves = []
    gathered_halves = []
    for h in range(2):
        lo = h * half_rows
        piece = jnp.where(col_index == 0, raw_panel[lo:lo + half_rows], 0.0)
        for k in range(1, col_count):
            pairs = [(r * col_count, r * col_count + k) for r in range(row_count)]
            start = k * piece_rows + lo
            piece = piece + lax.ppermute(
                raw_panel[start:start + half_rows], ("row", "col"), pairs
            )
        factor_half = jnp.dot(
            piece,
            panel_inverse.T,
            precision=lax.Precision.HIGHEST,
            preferred_element_type=jnp.float32,
        )
        factor_halves.append(factor_half)
        gathered_halves.append(lax.all_gather(factor_half, "col", axis=0, tiled=False))
    factor_piece = jnp.concatenate(factor_halves, axis=0)
    factor_panel = jnp.stack(gathered_halves, axis=1).reshape(height, PANEL)
    ratio = col_count // row_count
    pairs = [
        (r * col_count + k, (k % row_count) * col_count + r * ratio + k // row_count)
        for r in range(row_count)
        for k in range(col_count)
    ]
    moved = lax.ppermute(factor_piece, ("row", "col"), pairs)
    stack = [moved]
    for q in range(1, row_count):
        shift = [(r, (r + q) % row_count) for r in range(row_count)]
        stack.append(lax.ppermute(moved, "row", shift))
    order = (row_index - jnp.arange(row_count, dtype=jnp.int32)) % row_count
    across = jnp.take(jnp.stack(stack), order, axis=0).reshape(col_width, PANEL)
    update_term = lax.dot_general(
        factor_panel,
        across,
        (((1,), (1,)), ((), ())),
        precision=lax.Precision.HIGHEST,
        preferred_element_type=jnp.float32,
    )
    trailing = front_local - update_term
    return (factor_panel, trailing)


def solution(mesh):
    return jax.shard_map(
        on_device,
        mesh=mesh,
        in_specs=(P("col", "row"), P(), P("row"), P()),
        out_specs=(P("row", None), P("row", "col")),
        check_vma=False,
    )
```

```python
import jax
import jax.numpy as jnp
from jax import lax
from jax.sharding import PartitionSpec as P

F = 10240
M = 8192
BLK = 128
PANEL = 512


def on_device(updates, block_map, own_diag, panel_inverse):
    row_count = lax.axis_size("row")
    col_count = lax.axis_size("col")
    row_index = lax.axis_index("row")
    col_index = lax.axis_index("col")
    devices_all = row_count * col_count
    local_rows, local_cols = updates.shape
    row_items = local_rows // BLK
    col_items = local_cols // BLK
    half_cols = col_count // 2
    front_blocks = F // BLK
    front_rows = front_blocks // row_count
    front_cols = front_blocks // col_count
    height = front_rows * BLK
    col_width = front_cols * BLK
    block_map = block_map.astype(jnp.int32)
    child = col_index // half_cols
    child_map = jnp.take(block_map, child, axis=0)
    row_parent = lax.dynamic_slice_in_dim(child_map, col_index % half_cols * row_items, row_items)
    col_parent = lax.dynamic_slice_in_dim(child_map, row_index * col_items, col_items)
    inv_k = (
        jnp.zeros((row_count,), jnp.int32)
        .at[row_parent // front_rows]
        .set(jnp.arange(row_items, dtype=jnp.int32))
    )
    inv_l = (
        jnp.full((col_count,), -1, jnp.int32)
        .at[col_parent // front_cols]
        .set(jnp.arange(col_items, dtype=jnp.int32))
    )
    local_tiles = (
        updates.reshape(row_items, BLK, col_items, BLK)
        .transpose(0, 2, 1, 3)
        .reshape(row_items * col_items, BLK, BLK)
    )
    slot_tile = jnp.where(
        (inv_l >= 0)[None, :], inv_k[:, None] * col_items + inv_l[None, :], row_items * col_items
    )
    local_tiles = jnp.concatenate([local_tiles, jnp.zeros((1, BLK, BLK), jnp.float32)], axis=0)
    outgoing = jnp.take(local_tiles, slot_tile.reshape(-1), axis=0, mode="clip").reshape(
        devices_all, 1, BLK, BLK
    )
    incoming = lax.all_to_all(
        outgoing, ("row", "col"), split_axis=0, concat_axis=0, tiled=True
    ).reshape(devices_all, BLK, BLK)
    my_rows = row_index * front_rows + jnp.arange(front_rows, dtype=jnp.int32)
    my_cols = col_index * front_cols + jnp.arange(front_cols, dtype=jnp.int32)
    sources = []
    for child_id in range(2):
        inverse = (
            jnp.full((front_blocks,), -1, jnp.int32)
            .at[block_map[child_id]]
            .set(jnp.arange(block_map.shape[1], dtype=jnp.int32))
        )
        a = jnp.take(inverse, my_rows)
        b = jnp.take(inverse, my_cols)
        source = (jnp.maximum(b, 0) // col_items)[None, :] * col_count + (
            child_id * half_cols + jnp.maximum(a, 0) // row_items
        )[:, None]
        valid = (a >= 0)[:, None] & (b >= 0)[None, :]
        sources.append(jnp.where(valid, source, devices_all))

    def assemble(width):
        total = None
        for source in sources:
            part = jnp.take(
                incoming, source[:, :width].reshape(-1), axis=0, mode="fill", fill_value=0.0
            )
            total = part if total is None else total + part
        return (
            total.reshape(front_rows, width, BLK, BLK)
            .transpose(0, 2, 1, 3)
            .reshape(height, width * BLK)
        )

    row_global = row_index * height + jnp.arange(height, dtype=jnp.int32)
    col_global = col_index * col_width + jnp.arange(col_width, dtype=jnp.int32)
    diag = jnp.where(row_global[:, None] == col_global[None, :], own_diag[:, None], 0.0)
    raw_panel = assemble(PANEL // BLK) + diag[:, :PANEL]
    front_local = assemble(front_cols) + diag
    piece_rows = height // col_count
    piece = jnp.where(col_index == 0, raw_panel[:piece_rows], 0.0)
    for k in range(1, col_count):
        pairs = [(r * col_count, r * col_count + k) for r in range(row_count)]
        piece = piece + lax.ppermute(
            raw_panel[k * piece_rows:(k + 1) * piece_rows], ("row", "col"), pairs
        )
    factor_piece = jnp.dot(
        piece,
        panel_inverse.T,
        precision=lax.Precision.HIGHEST,
        preferred_element_type=jnp.float32,
    )
    col_stack = [factor_piece]
    for q in range(1, col_count):
        shift = [(t, (t + q) % col_count) for t in range(col_count)]
        col_stack.append(lax.ppermute(factor_piece, "col", shift))
    col_order = (col_index - jnp.arange(col_count, dtype=jnp.int32)) % col_count
    factor_panel = jnp.take(jnp.stack(col_stack), col_order, axis=0).reshape(height, PANEL)
    ratio = col_count // row_count
    pairs = [
        (r * col_count + k, (k % row_count) * col_count + r * ratio + k // row_count)
        for r in range(row_count)
        for k in range(col_count)
    ]
    moved = lax.ppermute(factor_piece, ("row", "col"), pairs)
    stack = [moved]
    for q in range(1, row_count):
        shift = [(r, (r + q) % row_count) for r in range(row_count)]
        stack.append(lax.ppermute(moved, "row", shift))
    order = (row_index - jnp.arange(row_count, dtype=jnp.int32)) % row_count
    across = jnp.take(jnp.stack(stack), order, axis=0).reshape(col_width, PANEL)
    update_term = lax.dot_general(
        factor_panel,
        across,
        (((1,), (1,)), ((), ())),
        precision=lax.Precision.HIGHEST,
        preferred_element_type=jnp.float32,
    )
    trailing = front_local - update_term
    return (factor_panel, trailing)


def solution(mesh):
    return jax.shard_map(
        on_device,
        mesh=mesh,
        in_specs=(P("col", "row"), P(), P("row"), P()),
        out_specs=(P("row", None), P("row", "col")),
        check_vma=False,
    )
```

```python
import jax
import jax.numpy as jnp
from jax import lax
from jax.sharding import PartitionSpec as P

F = 10240
M = 8192
BLK = 128
PANEL = 512


def on_device(updates, block_map, own_diag, panel_inverse):
    row_count = lax.axis_size("row")
    col_count = lax.axis_size("col")
    row_index = lax.axis_index("row")
    col_index = lax.axis_index("col")
    devices_all = row_count * col_count
    local_rows, local_cols = updates.shape
    row_items = local_rows // BLK
    col_items = local_cols // BLK
    half_cols = col_count // 2
    front_blocks = F // BLK
    front_rows = front_blocks // row_count
    front_cols = front_blocks // col_count
    height = front_rows * BLK
    col_width = front_cols * BLK
    block_map = block_map.astype(jnp.int32)
    child = col_index // half_cols
    child_map = jnp.take(block_map, child, axis=0)
    row_parent = lax.dynamic_slice_in_dim(child_map, col_index % half_cols * row_items, row_items)
    col_parent = lax.dynamic_slice_in_dim(child_map, row_index * col_items, col_items)
    inv_k = (
        jnp.zeros((row_count,), jnp.int32)
        .at[row_parent // front_rows]
        .set(jnp.arange(row_items, dtype=jnp.int32))
    )
    inv_l = (
        jnp.full((col_count,), -1, jnp.int32)
        .at[col_parent // front_cols]
        .set(jnp.arange(col_items, dtype=jnp.int32))
    )
    local_tiles = (
        updates.reshape(row_items, BLK, col_items, BLK)
        .transpose(0, 2, 1, 3)
        .reshape(row_items * col_items, BLK, BLK)
    )
    slot_tile = jnp.where(
        (inv_l >= 0)[None, :], inv_k[:, None] * col_items + inv_l[None, :], row_items * col_items
    )
    local_tiles = jnp.concatenate([local_tiles, jnp.zeros((1, BLK, BLK), jnp.float32)], axis=0)
    outgoing = jnp.take(local_tiles, slot_tile.reshape(-1), axis=0, mode="clip").reshape(
        devices_all, 1, BLK, BLK
    )
    panel_blocks = PANEL // BLK
    is_panel = col_parent < panel_blocks
    panel_l = jnp.argmax(is_panel).astype(jnp.int32)
    panel_tile = jnp.where(
        jnp.any(is_panel), inv_k * col_items + panel_l, row_items * col_items
    )
    panel_out = jnp.take(local_tiles, panel_tile, axis=0, mode="clip")
    panel_in = lax.all_to_all(panel_out, "row", split_axis=0, concat_axis=0, tiled=True)
    incoming = lax.all_to_all(
        outgoing, ("row", "col"), split_axis=0, concat_axis=0, tiled=True
    ).reshape(devices_all, BLK, BLK)
    my_rows = row_index * front_rows + jnp.arange(front_rows, dtype=jnp.int32)
    my_cols = col_index * front_cols + jnp.arange(front_cols, dtype=jnp.int32)
    sources = []
    inverses = []
    for child_id in range(2):
        inverse = (
            jnp.full((front_blocks,), -1, jnp.int32)
            .at[block_map[child_id]]
            .set(jnp.arange(block_map.shape[1], dtype=jnp.int32))
        )
        inverses.append(inverse)
        a = jnp.take(inverse, my_rows)
        b = jnp.take(inverse, my_cols)
        source = (jnp.maximum(b, 0) // col_items)[None, :] * col_count + (
            child_id * half_cols + jnp.maximum(a, 0) // row_items
        )[:, None]
        valid = (a >= 0)[:, None] & (b >= 0)[None, :]
        sources.append(jnp.where(valid, source, devices_all))

    def assemble(width):
        total = None
        for source in sources:
            part = jnp.take(
                incoming, source[:, :width].reshape(-1), axis=0, mode="fill", fill_value=0.0
            )
            total = part if total is None else total + part
        return (
            total.reshape(front_rows, width, BLK, BLK)
            .transpose(0, 2, 1, 3)
            .reshape(height, width * BLK)
        )

    row_global = row_index * height + jnp.arange(height, dtype=jnp.int32)
    col_global = col_index * col_width + jnp.arange(col_width, dtype=jnp.int32)
    diag = jnp.where(row_global[:, None] == col_global[None, :], own_diag[:, None], 0.0)
    my_inverse = jnp.where(child == 0, inverses[0], inverses[1])
    panel_b = my_inverse[:panel_blocks]
    panel_src = jnp.where(panel_b >= 0, panel_b // col_items, row_count)
    panel_part = (
        jnp.take(panel_in, panel_src, axis=0, mode="fill", fill_value=0.0)
        .transpose(1, 0, 2)
        .reshape(BLK, PANEL)
    )
    panel_parts = lax.all_gather(panel_part, "col", axis=0, tiled=False)
    raw_panel = None
    for c in range(2):
        a = jnp.take(inverses[c], my_rows)
        holder = jnp.where(a >= 0, c * half_cols + a // row_items, col_count)
        part = jnp.take(panel_parts, holder, axis=0, mode="fill", fill_value=0.0)
        raw_panel = part if raw_panel is None else raw_panel + part
    raw_panel = raw_panel.reshape(height, PANEL) + jnp.where(
        row_global[:, None] == jnp.arange(PANEL, dtype=jnp.int32)[None, :], own_diag[:, None], 0.0
    )
    factor_panel = jnp.dot(
        raw_panel,
        panel_inverse.T,
        precision=lax.Precision.HIGHEST,
        preferred_element_type=jnp.float32,
    )
    front_local = assemble(front_cols) + diag
    piece_rows = height // col_count
    factor_piece = lax.dynamic_slice_in_dim(factor_panel, col_index * piece_rows, piece_rows, 0)
    ratio = col_count // row_count
    pairs = [
        (r * col_count + k, (k % row_count) * col_count + r * ratio + k // row_count)
        for r in range(row_count)
        for k in range(col_count)
    ]
    moved = lax.ppermute(factor_piece, ("row", "col"), pairs)
    stack = [moved]
    for q in range(1, row_count):
        shift = [(r, (r + q) % row_count) for r in range(row_count)]
        stack.append(lax.ppermute(moved, "row", shift))
    order = (row_index - jnp.arange(row_count, dtype=jnp.int32)) % row_count
    across = jnp.take(jnp.stack(stack), order, axis=0).reshape(col_width, PANEL)
    update_term = lax.dot_general(
        factor_panel,
        across,
        (((1,), (1,)), ((), ())),
        precision=lax.Precision.HIGHEST,
        preferred_element_type=jnp.float32,
    )
    trailing = front_local - update_term
    return (factor_panel, trailing)


def solution(mesh):
    return jax.shard_map(
        on_device,
        mesh=mesh,
        in_specs=(P("col", "row"), P(), P("row"), P()),
        out_specs=(P("row", None), P("row", "col")),
        check_vma=False,
    )
```

```python
import jax
import jax.numpy as jnp
from jax import lax
from jax.sharding import PartitionSpec as P

F = 10240
M = 8192
BLK = 128
PANEL = 512


def on_device(updates, block_map, own_diag, panel_inverse):
    row_count = lax.axis_size("row")
    col_count = lax.axis_size("col")
    row_index = lax.axis_index("row")
    col_index = lax.axis_index("col")
    devices_all = row_count * col_count
    local_rows, local_cols = updates.shape
    row_items = local_rows // BLK
    col_items = local_cols // BLK
    half_cols = col_count // 2
    front_blocks = F // BLK
    front_rows = front_blocks // row_count
    front_cols = front_blocks // col_count
    height = front_rows * BLK
    col_width = front_cols * BLK
    block_map = block_map.astype(jnp.int32)
    child = col_index // half_cols
    child_map = jnp.take(block_map, child, axis=0)
    row_parent = lax.dynamic_slice_in_dim(child_map, col_index % half_cols * row_items, row_items)
    col_parent = lax.dynamic_slice_in_dim(child_map, row_index * col_items, col_items)
    inv_k = (
        jnp.zeros((row_count,), jnp.int32)
        .at[row_parent // front_rows]
        .set(jnp.arange(row_items, dtype=jnp.int32))
    )
    inv_l = (
        jnp.full((col_count,), -1, jnp.int32)
        .at[col_parent // front_cols]
        .set(jnp.arange(col_items, dtype=jnp.int32))
    )
    local_tiles = (
        updates.reshape(row_items, BLK, col_items, BLK)
        .transpose(0, 2, 1, 3)
        .reshape(row_items * col_items, BLK, BLK)
    )
    slot_tile = jnp.where(
        (inv_l >= 0)[None, :], inv_k[:, None] * col_items + inv_l[None, :], row_items * col_items
    )
    local_tiles = jnp.concatenate([local_tiles, jnp.zeros((1, BLK, BLK), jnp.float32)], axis=0)
    outgoing = jnp.take(local_tiles, slot_tile.reshape(-1), axis=0, mode="clip").reshape(
        devices_all, 1, BLK, BLK
    )
    panel_blocks = PANEL // BLK
    is_panel = col_parent < panel_blocks
    panel_l = jnp.argmax(is_panel).astype(jnp.int32)
    panel_tile = jnp.where(
        jnp.any(is_panel), inv_k * col_items + panel_l, row_items * col_items
    )
    panel_out = jnp.take(local_tiles, panel_tile, axis=0, mode="clip")
    panel_in = lax.all_to_all(panel_out, "row", split_axis=0, concat_axis=0, tiled=True)
    incoming = lax.all_to_all(
        outgoing, ("row", "col"), split_axis=0, concat_axis=0, tiled=True
    ).reshape(devices_all, BLK, BLK)
    my_rows = row_index * front_rows + jnp.arange(front_rows, dtype=jnp.int32)
    my_cols = col_index * front_cols + jnp.arange(front_cols, dtype=jnp.int32)
    sources = []
    inverses = []
    for child_id in range(2):
        inverse = (
            jnp.full((front_blocks,), -1, jnp.int32)
            .at[block_map[child_id]]
            .set(jnp.arange(block_map.shape[1], dtype=jnp.int32))
        )
        inverses.append(inverse)
        a = jnp.take(inverse, my_rows)
        b = jnp.take(inverse, my_cols)
        source = (jnp.maximum(b, 0) // col_items)[None, :] * col_count + (
            child_id * half_cols + jnp.maximum(a, 0) // row_items
        )[:, None]
        valid = (a >= 0)[:, None] & (b >= 0)[None, :]
        sources.append(jnp.where(valid, source, devices_all))

    def assemble(width):
        total = None
        for source in sources:
            part = jnp.take(
                incoming, source[:, :width].reshape(-1), axis=0, mode="fill", fill_value=0.0
            )
            total = part if total is None else total + part
        return (
            total.reshape(front_rows, width, BLK, BLK)
            .transpose(0, 2, 1, 3)
            .reshape(height, width * BLK)
        )

    row_global = row_index * height + jnp.arange(height, dtype=jnp.int32)
    col_global = col_index * col_width + jnp.arange(col_width, dtype=jnp.int32)
    diag = jnp.where(row_global[:, None] == col_global[None, :], own_diag[:, None], 0.0)
    my_inverse = jnp.where(child == 0, inverses[0], inverses[1])
    panel_b = my_inverse[:panel_blocks]
    panel_src = jnp.where(panel_b >= 0, panel_b // col_items, row_count)
    panel_part = (
        jnp.take(panel_in, panel_src, axis=0, mode="fill", fill_value=0.0)
        .transpose(1, 0, 2)
        .reshape(BLK, PANEL)
    )
    panel_parts = lax.all_gather(panel_part, "col", axis=0, tiled=False)
    piece_rows = height // col_count
    first_row = col_index * piece_rows
    first_block = first_row // BLK
    raw_panel = None
    piece_pair = None
    for c in range(2):
        a = jnp.take(inverses[c], my_rows)
        holder = jnp.where(a >= 0, c * half_cols + a // row_items, col_count)
        pair_holder = jnp.take(
            holder, first_block + jnp.arange(2, dtype=jnp.int32), mode="fill", fill_value=col_count
        )
        pair = jnp.take(panel_parts, pair_holder, axis=0, mode="fill", fill_value=0.0)
        piece_pair = pair if piece_pair is None else piece_pair + pair
        part = jnp.take(panel_parts, holder, axis=0, mode="fill", fill_value=0.0)
        raw_panel = part if raw_panel is None else raw_panel + part
    piece_rows_global = row_index * height + first_row + jnp.arange(piece_rows, dtype=jnp.int32)
    raw_piece = lax.dynamic_slice_in_dim(
        piece_pair.reshape(2 * BLK, PANEL), first_row % BLK, piece_rows, 0
    ) + jnp.where(
        piece_rows_global[:, None] == jnp.arange(PANEL, dtype=jnp.int32)[None, :],
        lax.dynamic_slice_in_dim(own_diag, first_row, piece_rows)[:, None],
        0.0,
    )
    factor_piece = jnp.dot(
        raw_piece,
        panel_inverse.T,
        precision=lax.Precision.HIGHEST,
        preferred_element_type=jnp.float32,
    )
    raw_panel = raw_panel.reshape(height, PANEL) + jnp.where(
        row_global[:, None] == jnp.arange(PANEL, dtype=jnp.int32)[None, :], own_diag[:, None], 0.0
    )
    factor_panel = jnp.dot(
        raw_panel,
        panel_inverse.T,
        precision=lax.Precision.HIGHEST,
        preferred_element_type=jnp.float32,
    )
    incoming, factor_piece = lax.optimization_barrier((incoming, factor_piece))
    front_local = assemble(front_cols) + diag
    ratio = col_count // row_count
    pairs = [
        (r * col_count + k, (k % row_count) * col_count + r * ratio + k // row_count)
        for r in range(row_count)
        for k in range(col_count)
    ]
    moved = lax.ppermute(factor_piece, ("row", "col"), pairs)
    stack = [moved]
    for q in range(1, row_count):
        shift = [(r, (r + q) % row_count) for r in range(row_count)]
        stack.append(lax.ppermute(moved, "row", shift))
    order = (row_index - jnp.arange(row_count, dtype=jnp.int32)) % row_count
    across = jnp.take(jnp.stack(stack), order, axis=0).reshape(col_width, PANEL)
    update_term = lax.dot_general(
        factor_panel,
        across,
        (((1,), (1,)), ((), ())),
        precision=lax.Precision.HIGHEST,
        preferred_element_type=jnp.float32,
    )
    trailing = front_local - update_term
    return (factor_panel, trailing)


def solution(mesh):
    return jax.shard_map(
        on_device,
        mesh=mesh,
        in_specs=(P("col", "row"), P(), P("row"), P()),
        out_specs=(P("row", None), P("row", "col")),
        check_vma=False,
    )
```

```python
import jax
import jax.numpy as jnp
from jax import lax
from jax.sharding import PartitionSpec as P

F = 10240
M = 8192
BLK = 128
PANEL = 512


def on_device(updates, block_map, own_diag, panel_inverse):
    row_count = lax.axis_size("row")
    col_count = lax.axis_size("col")
    row_index = lax.axis_index("row")
    col_index = lax.axis_index("col")
    devices_all = row_count * col_count
    local_rows, local_cols = updates.shape
    row_items = local_rows // BLK
    col_items = local_cols // BLK
    half_cols = col_count // 2
    front_blocks = F // BLK
    front_rows = front_blocks // row_count
    front_cols = front_blocks // col_count
    height = front_rows * BLK
    col_width = front_cols * BLK
    block_map = block_map.astype(jnp.int32)
    child = col_index // half_cols
    child_map = jnp.take(block_map, child, axis=0)
    row_parent = lax.dynamic_slice_in_dim(child_map, col_index % half_cols * row_items, row_items)
    col_parent = lax.dynamic_slice_in_dim(child_map, row_index * col_items, col_items)
    inv_k = (
        jnp.zeros((row_count,), jnp.int32)
        .at[row_parent // front_rows]
        .set(jnp.arange(row_items, dtype=jnp.int32))
    )
    inv_l = (
        jnp.full((col_count,), -1, jnp.int32)
        .at[col_parent // front_cols]
        .set(jnp.arange(col_items, dtype=jnp.int32))
    )
    local_tiles = (
        updates.reshape(row_items, BLK, col_items, BLK)
        .transpose(0, 2, 1, 3)
        .reshape(row_items * col_items, BLK, BLK)
    )
    slot_tile = jnp.where(
        (inv_l >= 0)[None, :], inv_k[:, None] * col_items + inv_l[None, :], row_items * col_items
    )
    local_tiles = jnp.pad(local_tiles, ((0, 1), (0, 0), (0, 0)))
    outgoing = jnp.take(local_tiles, slot_tile.reshape(-1), axis=0, mode="clip").reshape(
        devices_all, 1, BLK, BLK
    )
    panel_blocks = PANEL // BLK
    is_panel = col_parent < panel_blocks
    panel_l = jnp.argmax(is_panel).astype(jnp.int32)
    panel_tile = jnp.where(
        jnp.any(is_panel), inv_k * col_items + panel_l, row_items * col_items
    )
    panel_out = jnp.take(local_tiles, panel_tile, axis=0, mode="clip")
    outgoing, panel_out = lax.optimization_barrier((outgoing, panel_out))
    panel_in = lax.all_to_all(panel_out, "row", split_axis=0, concat_axis=0, tiled=True)
    incoming = lax.all_to_all(
        outgoing, ("row", "col"), split_axis=0, concat_axis=0, tiled=True
    ).reshape(devices_all, BLK, BLK)
    my_rows = row_index * front_rows + jnp.arange(front_rows, dtype=jnp.int32)
    my_cols = col_index * front_cols + jnp.arange(front_cols, dtype=jnp.int32)
    sources = []
    inverses = []
    for child_id in range(2):
        inverse = (
            jnp.full((front_blocks,), -1, jnp.int32)
            .at[block_map[child_id]]
            .set(jnp.arange(block_map.shape[1], dtype=jnp.int32))
        )
        inverses.append(inverse)
        a = jnp.take(inverse, my_rows)
        b = jnp.take(inverse, my_cols)
        source = (jnp.maximum(b, 0) // col_items)[None, :] * col_count + (
            child_id * half_cols + jnp.maximum(a, 0) // row_items
        )[:, None]
        valid = (a >= 0)[:, None] & (b >= 0)[None, :]
        sources.append(jnp.where(valid, source, devices_all))

    def assemble(width):
        total = None
        for source in sources:
            part = jnp.take(
                incoming, source[:, :width].reshape(-1), axis=0, mode="fill", fill_value=0.0
            )
            total = part if total is None else total + part
        return (
            total.reshape(front_rows, width, BLK, BLK)
            .transpose(0, 2, 1, 3)
            .reshape(height, width * BLK)
        )

    row_global = row_index * height + jnp.arange(height, dtype=jnp.int32)
    col_global = col_index * col_width + jnp.arange(col_width, dtype=jnp.int32)
    diag = jnp.where(row_global[:, None] == col_global[None, :], own_diag[:, None], 0.0)
    my_inverse = jnp.where(child == 0, inverses[0], inverses[1])
    panel_b = my_inverse[:panel_blocks]
    panel_src = jnp.where(panel_b >= 0, panel_b // col_items, row_count)
    panel_part = (
        jnp.take(panel_in, panel_src, axis=0, mode="fill", fill_value=0.0)
        .transpose(1, 0, 2)
        .reshape(BLK, PANEL)
    )
    panel_parts = lax.all_gather(panel_part, "col", axis=0, tiled=False)
    raw_panel = None
    for c in range(2):
        a = jnp.take(inverses[c], my_rows)
        holder = jnp.where(a >= 0, c * half_cols + a // row_items, col_count)
        part = jnp.take(panel_parts, holder, axis=0, mode="fill", fill_value=0.0)
        raw_panel = part if raw_panel is None else raw_panel + part
    raw_panel = raw_panel.reshape(height, PANEL) + jnp.where(
        row_global[:, None] == jnp.arange(PANEL, dtype=jnp.int32)[None, :], own_diag[:, None], 0.0
    )
    factor_panel = jnp.dot(
        raw_panel,
        panel_inverse.T,
        precision=lax.Precision.HIGHEST,
        preferred_element_type=jnp.float32,
    )
    front_local = assemble(front_cols) + diag
    piece_rows = height // col_count
    factor_piece = lax.dynamic_slice_in_dim(factor_panel, col_index * piece_rows, piece_rows, 0)
    ratio = col_count // row_count
    pairs = [
        (r * col_count + k, (k % row_count) * col_count + r * ratio + k // row_count)
        for r in range(row_count)
        for k in range(col_count)
    ]
    moved = lax.ppermute(factor_piece, ("row", "col"), pairs)
    stack = [moved]
    for q in range(1, row_count):
        shift = [(r, (r + q) % row_count) for r in range(row_count)]
        stack.append(lax.ppermute(moved, "row", shift))
    order = (row_index - jnp.arange(row_count, dtype=jnp.int32)) % row_count
    across = jnp.take(jnp.stack(stack), order, axis=0).reshape(col_width, PANEL)
    update_term = lax.dot_general(
        factor_panel,
        across,
        (((1,), (1,)), ((), ())),
        precision=lax.Precision.HIGHEST,
        preferred_element_type=jnp.float32,
    )
    trailing = front_local - update_term
    return (factor_panel, trailing)


def solution(mesh):
    return jax.shard_map(
        on_device,
        mesh=mesh,
        in_specs=(P("col", "row"), P(), P("row"), P()),
        out_specs=(P("row", None), P("row", "col")),
        check_vma=False,
    )
```

```python
import jax
import jax.numpy as jnp
from jax import lax
from jax.sharding import PartitionSpec as P

F = 10240
M = 8192
BLK = 128
PANEL = 512


def on_device(updates, block_map, own_diag, panel_inverse):
    row_count = lax.axis_size("row")
    col_count = lax.axis_size("col")
    row_index = lax.axis_index("row")
    col_index = lax.axis_index("col")
    devices_all = row_count * col_count
    local_rows, local_cols = updates.shape
    row_items = local_rows // BLK
    col_items = local_cols // BLK
    half_cols = col_count // 2
    front_blocks = F // BLK
    front_rows = front_blocks // row_count
    front_cols = front_blocks // col_count
    height = front_rows * BLK
    col_width = front_cols * BLK
    block_map = block_map.astype(jnp.int32)
    child = col_index // half_cols
    child_map = jnp.take(block_map, child, axis=0)
    row_parent = lax.dynamic_slice_in_dim(child_map, col_index % half_cols * row_items, row_items)
    col_parent = lax.dynamic_slice_in_dim(child_map, row_index * col_items, col_items)
    inv_k = (
        jnp.zeros((row_count,), jnp.int32)
        .at[row_parent // front_rows]
        .set(jnp.arange(row_items, dtype=jnp.int32))
    )
    inv_l = (
        jnp.full((col_count,), -1, jnp.int32)
        .at[col_parent // front_cols]
        .set(jnp.arange(col_items, dtype=jnp.int32))
    )
    local_tiles = (
        updates.reshape(row_items, BLK, col_items, BLK)
        .transpose(0, 2, 1, 3)
        .reshape(row_items * col_items, BLK, BLK)
    )
    slot_tile = jnp.where(
        (inv_l >= 0)[None, :], inv_k[:, None] * col_items + inv_l[None, :], row_items * col_items
    )
    local_tiles = jnp.concatenate([local_tiles, jnp.zeros((1, BLK, BLK), jnp.float32)], axis=0)
    outgoing = jnp.take(local_tiles, slot_tile.reshape(-1), axis=0, mode="clip").reshape(
        devices_all, 1, BLK, BLK
    )
    panel_blocks = PANEL // BLK
    is_panel = col_parent < panel_blocks
    panel_l = jnp.argmax(is_panel).astype(jnp.int32)
    panel_tile = jnp.where(
        jnp.any(is_panel), inv_k * col_items + panel_l, row_items * col_items
    )
    panel_out = jnp.take(local_tiles, panel_tile, axis=0, mode="clip")
    panel_in = lax.all_to_all(panel_out, "row", split_axis=0, concat_axis=0, tiled=True)
    incoming = lax.all_to_all(
        outgoing, ("row", "col"), split_axis=0, concat_axis=0, tiled=True
    ).reshape(devices_all, BLK, BLK)
    my_rows = row_index * front_rows + jnp.arange(front_rows, dtype=jnp.int32)
    my_cols = col_index * front_cols + jnp.arange(front_cols, dtype=jnp.int32)
    sources = []
    inverses = []
    for child_id in range(2):
        inverse = (
            jnp.full((front_blocks,), -1, jnp.int32)
            .at[block_map[child_id]]
            .set(jnp.arange(block_map.shape[1], dtype=jnp.int32))
        )
        inverses.append(inverse)
        a = jnp.take(inverse, my_rows)
        b = jnp.take(inverse, my_cols)
        source = (jnp.maximum(b, 0) // col_items)[None, :] * col_count + (
            child_id * half_cols + jnp.maximum(a, 0) // row_items
        )[:, None]
        valid = (a >= 0)[:, None] & (b >= 0)[None, :]
        sources.append(jnp.where(valid, source, devices_all))

    def assemble(width):
        total = None
        for source in sources:
            part = jnp.take(
                incoming, source[:, :width].reshape(-1), axis=0, mode="fill", fill_value=0.0
            )
            total = part if total is None else total + part
        return (
            total.reshape(front_rows, width, BLK, BLK)
            .transpose(0, 2, 1, 3)
            .reshape(height, width * BLK)
        )

    row_global = row_index * height + jnp.arange(height, dtype=jnp.int32)
    col_global = col_index * col_width + jnp.arange(col_width, dtype=jnp.int32)
    diag = jnp.where(row_global[:, None] == col_global[None, :], own_diag[:, None], 0.0)
    my_inverse = jnp.where(child == 0, inverses[0], inverses[1])
    panel_b = my_inverse[:panel_blocks]
    panel_src = jnp.where(panel_b >= 0, panel_b // col_items, row_count)
    panel_part = (
        jnp.take(panel_in, panel_src, axis=0, mode="fill", fill_value=0.0)
        .transpose(1, 0, 2)
        .reshape(BLK, PANEL)
    )
    panel_parts = lax.all_to_all(
        jnp.broadcast_to(panel_part[None], (col_count, BLK, PANEL)),
        "col",
        split_axis=0,
        concat_axis=0,
        tiled=True,
    )
    raw_panel = None
    for c in range(2):
        a = jnp.take(inverses[c], my_rows)
        holder = jnp.where(a >= 0, c * half_cols + a // row_items, col_count)
        part = jnp.take(panel_parts, holder, axis=0, mode="fill", fill_value=0.0)
        raw_panel = part if raw_panel is None else raw_panel + part
    raw_panel = raw_panel.reshape(height, PANEL) + jnp.where(
        row_global[:, None] == jnp.arange(PANEL, dtype=jnp.int32)[None, :], own_diag[:, None], 0.0
    )
    factor_panel = jnp.dot(
        raw_panel,
        panel_inverse.T,
        precision=lax.Precision.HIGHEST,
        preferred_element_type=jnp.float32,
    )
    front_local = assemble(front_cols) + diag
    piece_rows = height // col_count
    factor_piece = lax.dynamic_slice_in_dim(factor_panel, col_index * piece_rows, piece_rows, 0)
    ratio = col_count // row_count
    pairs = [
        (r * col_count + k, (k % row_count) * col_count + r * ratio + k // row_count)
        for r in range(row_count)
        for k in range(col_count)
    ]
    moved = lax.ppermute(factor_piece, ("row", "col"), pairs)
    stack = [moved]
    for q in range(1, row_count):
        shift = [(r, (r + q) % row_count) for r in range(row_count)]
        stack.append(lax.ppermute(moved, "row", shift))
    order = (row_index - jnp.arange(row_count, dtype=jnp.int32)) % row_count
    across = jnp.take(jnp.stack(stack), order, axis=0).reshape(col_width, PANEL)
    update_term = lax.dot_general(
        factor_panel,
        across,
        (((1,), (1,)), ((), ())),
        precision=lax.Precision.HIGHEST,
        preferred_element_type=jnp.float32,
    )
    trailing = front_local - update_term
    return (factor_panel, trailing)


def solution(mesh):
    return jax.shard_map(
        on_device,
        mesh=mesh,
        in_specs=(P("col", "row"), P(), P("row"), P()),
        out_specs=(P("row", None), P("row", "col")),
        check_vma=False,
    )
```

```python
import jax
import jax.numpy as jnp
from jax import lax
from jax.sharding import PartitionSpec as P

F = 10240
M = 8192
BLK = 128
PANEL = 512


def on_device(updates, block_map, own_diag, panel_inverse):
    row_count = lax.axis_size("row")
    col_count = lax.axis_size("col")
    row_index = lax.axis_index("row")
    col_index = lax.axis_index("col")
    devices_all = row_count * col_count
    local_rows, local_cols = updates.shape
    row_items = local_rows // BLK
    col_items = local_cols // BLK
    half_cols = col_count // 2
    front_blocks = F // BLK
    front_rows = front_blocks // row_count
    front_cols = front_blocks // col_count
    height = front_rows * BLK
    col_width = front_cols * BLK
    block_map = block_map.astype(jnp.int32)
    child = col_index // half_cols
    child_map = jnp.take(block_map, child, axis=0)
    row_parent = lax.dynamic_slice_in_dim(child_map, col_index % half_cols * row_items, row_items)
    col_parent = lax.dynamic_slice_in_dim(child_map, row_index * col_items, col_items)
    inv_k = (
        jnp.zeros((row_count,), jnp.int32)
        .at[row_parent // front_rows]
        .set(jnp.arange(row_items, dtype=jnp.int32))
    )
    inv_l = (
        jnp.full((col_count,), -1, jnp.int32)
        .at[col_parent // front_cols]
        .set(jnp.arange(col_items, dtype=jnp.int32))
    )
    local_tiles = (
        updates.reshape(row_items, BLK, col_items, BLK)
        .transpose(0, 2, 1, 3)
        .reshape(row_items * col_items, BLK, BLK)
    )
    slot_tile = jnp.where(
        (inv_l >= 0)[None, :], inv_k[:, None] * col_items + inv_l[None, :], row_items * col_items
    )
    local_tiles = jnp.concatenate([local_tiles, jnp.zeros((1, BLK, BLK), jnp.float32)], axis=0)
    outgoing = jnp.take(local_tiles, slot_tile.reshape(-1), axis=0, mode="clip").reshape(
        devices_all, 1, BLK, BLK
    )
    panel_blocks = PANEL // BLK
    is_panel = col_parent < panel_blocks
    panel_l = jnp.argmax(is_panel).astype(jnp.int32)
    panel_tile = jnp.where(
        jnp.any(is_panel), inv_k * col_items + panel_l, row_items * col_items
    )
    panel_out = jnp.take(local_tiles, panel_tile, axis=0, mode="clip")
    panel_in = lax.all_to_all(panel_out, "row", split_axis=0, concat_axis=0, tiled=True)
    incoming = lax.all_to_all(
        outgoing, ("row", "col"), split_axis=0, concat_axis=0, tiled=True
    ).reshape(devices_all, BLK, BLK)
    my_rows = row_index * front_rows + jnp.arange(front_rows, dtype=jnp.int32)
    my_cols = col_index * front_cols + jnp.arange(front_cols, dtype=jnp.int32)
    sources = []
    inverses = []
    for child_id in range(2):
        inverse = (
            jnp.full((front_blocks,), -1, jnp.int32)
            .at[block_map[child_id]]
            .set(jnp.arange(block_map.shape[1], dtype=jnp.int32))
        )
        inverses.append(inverse)
        a = jnp.take(inverse, my_rows)
        b = jnp.take(inverse, my_cols)
        source = (jnp.maximum(b, 0) // col_items)[None, :] * col_count + (
            child_id * half_cols + jnp.maximum(a, 0) // row_items
        )[:, None]
        valid = (a >= 0)[:, None] & (b >= 0)[None, :]
        sources.append(jnp.where(valid, source, devices_all))

    def assemble(width):
        total = None
        for source in sources:
            part = jnp.take(
                incoming, source[:, :width].reshape(-1), axis=0, mode="fill", fill_value=0.0
            )
            total = part if total is None else total + part
        return (
            total.reshape(front_rows, width, BLK, BLK)
            .transpose(0, 2, 1, 3)
            .reshape(height, width * BLK)
        )

    row_global = row_index * height + jnp.arange(height, dtype=jnp.int32)
    col_global = col_index * col_width + jnp.arange(col_width, dtype=jnp.int32)
    diag = jnp.where(row_global[:, None] == col_global[None, :], own_diag[:, None], 0.0)
    my_inverse = jnp.where(child == 0, inverses[0], inverses[1])
    panel_b = my_inverse[:panel_blocks]
    panel_src = jnp.where(panel_b >= 0, panel_b // col_items, row_count)
    panel_part = (
        jnp.take(panel_in, panel_src, axis=0, mode="fill", fill_value=0.0)
        .transpose(1, 0, 2)
        .reshape(BLK, PANEL)
    )
    panel_parts = lax.all_gather(panel_part, "col", axis=0, tiled=False)
    raw_panel = None
    for c in range(2):
        a = jnp.take(inverses[c], my_rows)
        holder = jnp.where(a >= 0, c * half_cols + a // row_items, col_count)
        part = jnp.take(panel_parts, holder, axis=0, mode="fill", fill_value=0.0)
        raw_panel = part if raw_panel is None else raw_panel + part
    raw_panel = raw_panel.reshape(height, PANEL) + jnp.where(
        row_global[:, None] == jnp.arange(PANEL, dtype=jnp.int32)[None, :], own_diag[:, None], 0.0
    )
    factor_panel = jnp.dot(
        raw_panel,
        panel_inverse.T,
        precision=lax.Precision.HIGHEST,
        preferred_element_type=jnp.float32,
    )
    front_local = assemble(front_cols) + diag
    piece_rows = height // col_count
    factor_piece = lax.dynamic_slice_in_dim(factor_panel, col_index * piece_rows, piece_rows, 0)
    ratio = col_count // row_count
    pairs = [
        (r * col_count + k, (k % row_count) * col_count + r * ratio + k // row_count)
        for r in range(row_count)
        for k in range(col_count)
    ]
    moved = lax.ppermute(factor_piece, ("row", "col"), pairs)
    stack = [moved]
    for q in range(1, row_count):
        shift = [(r, (r + q) % row_count) for r in range(row_count)]
        stack.append(lax.ppermute(moved, "row", shift))
    chunk = col_width // row_count
    trailing = front_local
    for q in range(row_count):
        offset = ((row_index - q) % row_count) * chunk
        update_term = lax.dot_general(
            factor_panel,
            stack[q],
            (((1,), (1,)), ((), ())),
            precision=lax.Precision.HIGHEST,
            preferred_element_type=jnp.float32,
        )
        current = lax.dynamic_slice_in_dim(front_local, offset, chunk, 1)
        trailing = lax.dynamic_update_slice_in_dim(trailing, current - update_term, offset, 1)
    return (factor_panel, trailing)


def solution(mesh):
    return jax.shard_map(
        on_device,
        mesh=mesh,
        in_specs=(P("col", "row"), P(), P("row"), P()),
        out_specs=(P("row", None), P("row", "col")),
        check_vma=False,
    )
```

```python
import jax
import jax.numpy as jnp
from jax import lax
from jax.sharding import PartitionSpec as P

F = 10240
M = 8192
BLK = 128
PANEL = 512


def on_device(updates, block_map, own_diag, panel_inverse):
    row_count = lax.axis_size("row")
    col_count = lax.axis_size("col")
    row_index = lax.axis_index("row")
    col_index = lax.axis_index("col")
    devices_all = row_count * col_count
    local_rows, local_cols = updates.shape
    row_items = local_rows // BLK
    col_items = local_cols // BLK
    half_cols = col_count // 2
    front_blocks = F // BLK
    front_rows = front_blocks // row_count
    front_cols = front_blocks // col_count
    height = front_rows * BLK
    col_width = front_cols * BLK
    block_map = block_map.astype(jnp.int32)
    child = col_index // half_cols
    child_map = jnp.take(block_map, child, axis=0)
    row_parent = lax.dynamic_slice_in_dim(child_map, col_index % half_cols * row_items, row_items)
    col_parent = lax.dynamic_slice_in_dim(child_map, row_index * col_items, col_items)
    inv_k = (
        jnp.zeros((row_count,), jnp.int32)
        .at[row_parent // front_rows]
        .set(jnp.arange(row_items, dtype=jnp.int32))
    )
    inv_l = (
        jnp.full((col_count,), -1, jnp.int32)
        .at[col_parent // front_cols]
        .set(jnp.arange(col_items, dtype=jnp.int32))
    )
    local_tiles = (
        updates.reshape(row_items, BLK, col_items, BLK)
        .transpose(0, 2, 1, 3)
        .reshape(row_items * col_items, BLK, BLK)
    )
    slot_tile = jnp.where(
        (inv_l >= 0)[None, :], inv_k[:, None] * col_items + inv_l[None, :], row_items * col_items
    )
    local_tiles = jnp.concatenate([local_tiles, jnp.zeros((1, BLK, BLK), jnp.float32)], axis=0)
    outgoing = jnp.take(local_tiles, slot_tile.reshape(-1), axis=0, mode="clip").reshape(
        devices_all, 1, BLK, BLK
    )
    panel_blocks = PANEL // BLK
    is_panel = col_parent < panel_blocks
    panel_l = jnp.argmax(is_panel).astype(jnp.int32)
    panel_tile = jnp.where(
        jnp.any(is_panel), inv_k * col_items + panel_l, row_items * col_items
    )
    panel_out = jnp.take(local_tiles, panel_tile, axis=0, mode="clip")
    panel_in = lax.all_to_all(panel_out, "row", split_axis=0, concat_axis=0, tiled=True)
    incoming = lax.all_to_all(
        outgoing, ("row", "col"), split_axis=0, concat_axis=0, tiled=True
    ).reshape(devices_all, BLK, BLK)
    my_rows = row_index * front_rows + jnp.arange(front_rows, dtype=jnp.int32)
    my_cols = col_index * front_cols + jnp.arange(front_cols, dtype=jnp.int32)
    sources = []
    inverses = []
    for child_id in range(2):
        inverse = (
            jnp.full((front_blocks,), -1, jnp.int32)
            .at[block_map[child_id]]
            .set(jnp.arange(block_map.shape[1], dtype=jnp.int32))
        )
        inverses.append(inverse)
        a = jnp.take(inverse, my_rows)
        b = jnp.take(inverse, my_cols)
        source = (jnp.maximum(b, 0) // col_items)[None, :] * col_count + (
            child_id * half_cols + jnp.maximum(a, 0) // row_items
        )[:, None]
        valid = (a >= 0)[:, None] & (b >= 0)[None, :]
        sources.append(jnp.where(valid, source, devices_all))

    def assemble(width):
        total = None
        for source in sources:
            part = jnp.take(
                incoming, source[:, :width].reshape(-1), axis=0, mode="fill", fill_value=0.0
            )
            total = part if total is None else total + part
        return (
            total.reshape(front_rows, width, BLK, BLK)
            .transpose(0, 2, 1, 3)
            .reshape(height, width * BLK)
        )

    row_global = row_index * height + jnp.arange(height, dtype=jnp.int32)
    col_global = col_index * col_width + jnp.arange(col_width, dtype=jnp.int32)
    diag = jnp.where(row_global[:, None] == col_global[None, :], own_diag[:, None], 0.0)
    my_inverse = jnp.where(child == 0, inverses[0], inverses[1])
    panel_b = my_inverse[:panel_blocks]
    panel_src = jnp.where(panel_b >= 0, panel_b // col_items, row_count)
    panel_part = (
        jnp.take(panel_in, panel_src, axis=0, mode="fill", fill_value=0.0)
        .transpose(1, 0, 2)
        .reshape(BLK, PANEL)
    )
    panel_parts = lax.all_gather(panel_part, "col", axis=0, tiled=False)
    raw_panel = None
    for c in range(2):
        a = jnp.take(inverses[c], my_rows)
        holder = jnp.where(a >= 0, c * half_cols + a // row_items, col_count)
        part = jnp.take(panel_parts, holder, axis=0, mode="fill", fill_value=0.0)
        raw_panel = part if raw_panel is None else raw_panel + part
    raw_panel = raw_panel.reshape(height, PANEL) + jnp.where(
        row_global[:, None] == jnp.arange(PANEL, dtype=jnp.int32)[None, :], own_diag[:, None], 0.0
    )
    factor_panel = jnp.dot(
        raw_panel,
        panel_inverse.T,
        precision=lax.Precision.HIGHEST,
        preferred_element_type=jnp.float32,
    )
    incoming, factor_panel = lax.optimization_barrier((incoming, factor_panel))
    front_local = assemble(front_cols) + diag
    piece_rows = height // col_count
    factor_piece = lax.dynamic_slice_in_dim(factor_panel, col_index * piece_rows, piece_rows, 0)
    ratio = col_count // row_count
    pairs = [
        (r * col_count + k, (k % row_count) * col_count + r * ratio + k // row_count)
        for r in range(row_count)
        for k in range(col_count)
    ]
    moved = lax.ppermute(factor_piece, ("row", "col"), pairs)
    stack = [moved]
    for q in range(1, row_count):
        shift = [(r, (r + q) % row_count) for r in range(row_count)]
        stack.append(lax.ppermute(moved, "row", shift))
    order = (row_index - jnp.arange(row_count, dtype=jnp.int32)) % row_count
    across = jnp.take(jnp.stack(stack), order, axis=0).reshape(col_width, PANEL)
    update_term = lax.dot_general(
        factor_panel,
        across,
        (((1,), (1,)), ((), ())),
        precision=lax.Precision.HIGHEST,
        preferred_element_type=jnp.float32,
    )
    trailing = front_local - update_term
    return (factor_panel, trailing)


def solution(mesh):
    return jax.shard_map(
        on_device,
        mesh=mesh,
        in_specs=(P("col", "row"), P(), P("row"), P()),
        out_specs=(P("row", None), P("row", "col")),
        check_vma=False,
    )
```
